128 devices in a mesh: space: 16 (over x, y_hi, core), tm: 8 (over z, y_lo).
Axes of the slice: x: 4, y: 4 (y_hi: 2, y_lo: 2; y = y_hi * 2 + y_lo), z: 4, core: 2. Of those that a mesh axis runs over, the one named last changes fastest.
Arguments:
- source_snap: bfloat16 [32, 128, 64, 8, 256], P('space', 'tm'), may hold values from -1.796875 to 1.796875
- receiver_snap: bfloat16 [32, 128, 64, 8, 256], P('space', 'tm'), may hold values from -1.796875 to 1.796875
- start_tile: int32 [32], P('space'), may hold values from 0 to 14, as said below
Outputs:
- model_image: float32 [8, 64, 33, 2048], P('tm', None, None, 'space')
The draws below stay inside these ranges and needn't reach their ends.
Inputs may be any that keep to these rules, and one draw needn't show every extreme that they name: `start_tile`: A shot held by index i of space (shots i * 2 to (i+1) * 2 - 1) has its first tile at i - 1 or i, limited to 0 .. 14; of the first two shots of each index, one is placed at i - 1 and the other at i before that limit.
All inputs are finite; a program needn't handle non-finite values.
Results may differ from the reference program's by a relative error of at most 0.0003.
Values may be sent and summed in bfloat16 or wider, within the bound.
No kernel may reach another device: no remote copies, remote signals or barrier semaphores. Data moves between devices by JAX's collectives and lax.ppermute only.
A program may use at most 128 MiB of HBM per device.

```python
import jax
import jax.numpy as jnp
from jax import lax

C = 64
LAGS = 33
TILE = 128
STEPS = 128
SHOT_DEV = 2
APX = 256
SHOTS = 32
DEPTH = 8
TILES = 16
MX = 2048
N_SPACE = 16


def draw_start_tile(key, part):
    holder = jnp.arange(SHOTS, dtype=jnp.int32) // SHOT_DEV
    local = jnp.arange(SHOTS, dtype=jnp.int32) % SHOT_DEV
    first_key = jax.random.fold_in(key, 11)
    rest_key = jax.random.fold_in(key, 23)
    flip = jax.random.randint(first_key, (N_SPACE,), 0, 2, dtype=jnp.int32)
    flip_shot = jnp.repeat(flip, SHOT_DEV)
    other = jax.random.randint(rest_key, (SHOTS,), 0, 2, dtype=jnp.int32)
    offset = jnp.where(local == 0, flip_shot, jnp.where(local == 1, 1 - flip_shot, other))
    return jnp.clip(holder - offset, 0, TILES - 2).astype(jnp.int32)


def levels(stream_key, dims, cuts, low, largest):
    gain = 1.0
    for position, blocks in cuts:
        heights = jax.random.uniform(jax.random.fold_in(jax.random.fold_in(stream_key, 6), position), (blocks,), jnp.float32, low / len(cuts), largest / len(cuts))
        gain = gain * jnp.repeat(jnp.exp(heights), dims[position] // blocks).reshape((-1,) + (1,) * (len(dims) - 1 - position))
    return gain


def scatter_about(own_key, extent, scale, most, cuts=(), kind=jnp.bfloat16):
    result = scale * jax.random.normal(own_key, extent, jnp.float32)
    if cuts:
        result = result * levels(own_key, extent, cuts, -0.22, 0.18)
    return jnp.clip(result, -most, most).astype(kind)


def setup_inputs(seed: int = 0) -> dict:
    seeds = jax.random.split(jax.random.key(seed), 4)
    return {
        "source_snap": scatter_about(seeds[0], (SHOTS, STEPS, C, DEPTH, APX), 0.3, 1.796875, ((0, 16), (1, 8))),
        "receiver_snap": scatter_about(seeds[1], (SHOTS, STEPS, C, DEPTH, APX), 0.3, 1.796875, ((0, 16), (1, 8))),
        "start_tile": draw_start_tile(jax.random.fold_in(seeds[3], 71), 0),
    }


def shot_image(src, rec):
    half = (LAGS - 1) // 2
    src_pad = jnp.pad(src.astype(jnp.float32), ((0, 0), (0, 0), (0, 0), (half, half)))
    rec_pad = jnp.pad(rec.astype(jnp.float32), ((0, 0), (0, 0), (0, 0), (half, half)))
    width = src.shape[3]
    planes = []
    for lag in range(LAGS):
        shift_by = lag - half
        left = src_pad[:, :, :, half - shift_by:half - shift_by + width]
        right = rec_pad[:, :, :, half + shift_by:half + shift_by + width]
        planes.append(jnp.einsum("tczx,tczx->zcx", left, right))
    return jnp.stack(planes, axis=2)


def reference(source_snap, receiver_snap, start_tile):
    model_init = jnp.zeros((DEPTH, C, LAGS, MX), jnp.float32)

    def add_shot(model_now, inputs):
        src, rec, first = inputs
        image = shot_image(src, rec)
        column = (first * TILE).astype(jnp.int32)
        zero = jnp.zeros((), jnp.int32)
        old = lax.dynamic_slice(model_now, (zero, zero, zero, column), image.shape)
        return lax.dynamic_update_slice(model_now, old + image, (zero, zero, zero, column)), None

    model_image, _ = lax.scan(add_shot, model_init, (source_snap, receiver_snap, start_tile))
    return model_image
```

```python
import functools

import jax
import jax.numpy as jnp
from jax import lax
from jax.experimental import pallas as pl
from jax.experimental.pallas import tpu as pltpu
from jax.sharding import PartitionSpec as P

LAGS = 33
TILE = 128
CB = 8


def passed_along(block, axis, distance):
    devices = range(lax.axis_size(axis))
    route = [(i - distance, i) for i in devices if i - distance in devices]
    return lax.ppermute(block, axis, route)


def lag_kernel(s_ref, r_ref, o_ref, band_ref):
    src, _, cb, t16, width = s_ref.shape
    half = (LAGS - 1) // 2
    rows = band_ref.shape[0]
    u_i = lax.broadcasted_iota(jnp.int32, (width, width), 0)
    k_i = lax.broadcasted_iota(jnp.int32, (width, width), 1)
    v_ok = (u_i - k_i + 2 * half >= 0) & (u_i - k_i + 2 * half < width)
    x_i = lax.broadcasted_iota(jnp.int32, (1, width), 1)

    def one_channel(c, carry):
        s_t = s_ref[:, 0, c, :, :].reshape(src * t16, width)
        r_t = r_ref[:, 0, c, :, :].reshape(src * t16, width)
        g = lax.dot_general(s_t, r_t, (((0,), (0,)), ((), ())),
                            preferred_element_type=jnp.float32)
        q = pltpu.roll(g, 2 * half + 1, 1, stride=1, stride_axis=0)
        q = jnp.where(v_ok, q, 0.0)
        band_ref[...] = q[:, :TILE].T[:rows, :]
        for j in range(LAGS):
            d = half - j
            w = band_ref[2 * j:2 * j + 1, :]
            out = pltpu.roll(w, d % width, 1)
            out = jnp.where((x_i - d >= 0) & (x_i - d < width), out, 0.0)
            o_ref[0, c, pl.ds(half + d, 1), :] = out
        return carry

    lax.fori_loop(0, cb, one_channel, 0)


def lag_images(src, rec):
    n_src, shots, chans, t16, width = src.shape
    in_spec = pl.BlockSpec((n_src, 1, CB, t16, width), lambda i, j: (0, i, j, 0, 0))
    return pl.pallas_call(
        lag_kernel,
        grid=(shots, chans // CB),
        in_specs=[in_spec, in_spec],
        out_specs=pl.BlockSpec((1, CB, LAGS, width), lambda i, j: (i, j, 0, 0)),
        out_shape=jax.ShapeDtypeStruct((shots, chans, LAGS, width), jnp.float32),
        scratch_shapes=[pltpu.VMEM((72, width), jnp.float32)],
    )(src, rec)


def place_tiles(image, first, base, slots):
    shots, chans, lags, width = image.shape
    blocks = image.reshape(shots, chans, lags, 2, TILE)
    target = first[:, None] + jnp.arange(2, dtype=jnp.int32)[None, :] - base
    out = []
    for k in range(slots):
        acc = None
        for s in range(shots):
            for a in range(2):
                term = jnp.where(target[s, a] == k, blocks[s, :, :, a, :], 0.0)
                acc = term if acc is None else acc + term
        out.append(acc)
    return out


def body(source_snap, receiver_snap, start_tile):
    def moved(x, flip=False):
        if flip:
            x = jnp.flip(x, axis=4)
        x = jnp.transpose(x, (3, 0, 2, 1, 4))
        return lax.all_to_all(x, "tm", split_axis=0, concat_axis=0, tiled=True)

    image = lag_images(moved(source_snap), moved(receiver_snap, True))
    owner = lax.axis_index("space")
    placed = place_tiles(image, start_tile, owner - 1, 3)
    own_part = placed[1]
    right_part = passed_along(placed[0], "space", -1)
    left_part = passed_along(placed[2], "space", 1)
    return (own_part + right_part + left_part)[None]


def solution(mesh):
    in_specs = (P("space", "tm", None, None, None), P("space", "tm", None, None, None), P("space"))
    out_specs = P("tm", None, None, "space")
    return jax.shard_map(body, mesh=mesh, in_specs=in_specs, out_specs=out_specs, check_vma=False)
```

```python
import functools

import jax
import jax.numpy as jnp
from jax import lax
from jax.experimental import pallas as pl
from jax.experimental.pallas import tpu as pltpu
from jax.sharding import PartitionSpec as P

LAGS = 33
TILE = 128
CB = 8
NCH = 4


def passed_along(block, axis, distance):
    devices = range(lax.axis_size(axis))
    route = [(i - distance, i) for i in devices if i - distance in devices]
    return lax.ppermute(block, axis, route)


def lag_kernel(x_ref, o_ref, band_ref):
    src, _, _, cb, t16, width = x_ref.shape
    half = (LAGS - 1) // 2
    rows = band_ref.shape[0]
    u_i = lax.broadcasted_iota(jnp.int32, (width, width), 0)
    k_i = lax.broadcasted_iota(jnp.int32, (width, width), 1)
    v_ok = (u_i - k_i + 2 * half >= 0) & (u_i - k_i + 2 * half < width)
    flip = jnp.where(u_i + k_i == width - 1, 1.0, 0.0).astype(jnp.bfloat16)
    x_i = lax.broadcasted_iota(jnp.int32, (1, width), 1)

    def one_channel(c, carry):
        s_t = x_ref[:, 0, 0, c, :, :].reshape(src * t16, width)
        r_t = x_ref[:, 1, 0, c, :, :].reshape(src * t16, width)
        r_f = jnp.dot(r_t, flip, preferred_element_type=jnp.float32).astype(jnp.bfloat16)
        g = lax.dot_general(s_t, r_f, (((0,), (0,)), ((), ())),
                            preferred_element_type=jnp.float32)
        q = pltpu.roll(g, 2 * half + 1, 1, stride=1, stride_axis=0)
        q = jnp.where(v_ok, q, 0.0)
        band_ref[...] = q[:, :TILE].T[:rows, :]
        for j in range(LAGS):
            d = half - j
            w = band_ref[2 * j:2 * j + 1, :]
            out = pltpu.roll(w, d % width, 1)
            out = jnp.where((x_i - d >= 0) & (x_i - d < width), out, 0.0)
            o_ref[0, 0, c, pl.ds(half + d, 1), :] = out[:, :TILE]
            o_ref[0, 1, c, pl.ds(half + d, 1), :] = out[:, TILE:]
        return carry

    lax.fori_loop(0, cb, one_channel, 0)


def lag_images(pair):
    n_src, _, shots, chans, t16, width = pair.shape
    cb = min(CB, chans)
    return pl.pallas_call(
        lag_kernel,
        grid=(shots, chans // cb),
        in_specs=[pl.BlockSpec((n_src, 2, 1, cb, t16, width), lambda i, j: (0, 0, i, j, 0, 0))],
        out_specs=pl.BlockSpec((1, 2, cb, LAGS, TILE), lambda i, j: (i, 0, j, 0, 0)),
        out_shape=jax.ShapeDtypeStruct((shots, 2, chans, LAGS, TILE), jnp.float32),
        scratch_shapes=[pltpu.VMEM((72, width), jnp.float32)],
    )(pair)


def place_tiles(image, first, base, slots):
    shots = image.shape[0]
    target = first[:, None] + jnp.arange(2, dtype=jnp.int32)[None, :] - base
    out = []
    for k in range(slots):
        acc = None
        for s in range(shots):
            for a in range(2):
                term = jnp.where(target[s, a] == k, image[s, a], 0.0)
                acc = term if acc is None else acc + term
        out.append(acc)
    return out


def body(source_snap, receiver_snap, start_tile):
    chans = source_snap.shape[2]
    owner = lax.axis_index("space")
    parts = []
    images = []
    for g in range(NCH):
        cs = slice(g * chans // NCH, (g + 1) * chans // NCH)
        pair = jnp.stack([source_snap[:, :, cs], receiver_snap[:, :, cs]])
        pair = jnp.transpose(pair, (4, 0, 1, 3, 2, 5))
        if g >= 2:
            pair, images[g - 2] = lax.optimization_barrier((pair, images[g - 2]))
        pair = lax.all_to_all(pair, "tm", split_axis=0, concat_axis=0, tiled=True)
        images.append(lag_images(pair))
    for image in images:
        placed = place_tiles(image, start_tile, owner - 1, 3)
        right_part = passed_along(placed[0], "space", -1)
        left_part = passed_along(placed[2], "space", 1)
        parts.append(placed[1] + right_part + left_part)
    return jnp.concatenate(parts, axis=0)[None]


def solution(mesh):
    in_specs = (P("space", "tm", None, None, None), P("space", "tm", None, None, None), P("space"))
    out_specs = P("tm", None, None, "space")
    return jax.shard_map(body, mesh=mesh, in_specs=in_specs, out_specs=out_specs, check_vma=False)
```

```python
import functools

import jax
import jax.numpy as jnp
from jax import lax
from jax.experimental import pallas as pl
from jax.experimental.pallas import tpu as pltpu
from jax.sharding import PartitionSpec as P

LAGS = 33
TILE = 128
CB = 8
CHUNKS = (48, 16)


def passed_along(block, axis, distance):
    devices = range(lax.axis_size(axis))
    route = [(i - distance, i) for i in devices if i - distance in devices]
    return lax.ppermute(block, axis, route)


def lag_kernel(x_ref, o_ref, band_ref):
    src, _, _, cb, t16, width = x_ref.shape
    half = (LAGS - 1) // 2
    rows = band_ref.shape[0]
    u_i = lax.broadcasted_iota(jnp.int32, (width, width), 0)
    k_i = lax.broadcasted_iota(jnp.int32, (width, width), 1)
    v_ok = (u_i - k_i + 2 * half >= 0) & (u_i - k_i + 2 * half < width)
    x_i = lax.broadcasted_iota(jnp.int32, (1, width), 1)

    def one_channel(c, carry):
        s_t = x_ref[:, 0, 0, c, :, :].reshape(src * t16, width)
        r_t = x_ref[:, 1, 0, c, :, :].reshape(src * t16, width)
        g = lax.dot_general(s_t, r_t, (((0,), (0,)), ((), ())),
                            preferred_element_type=jnp.float32)
        q = pltpu.roll(g, 2 * half + 1, 1, stride=1, stride_axis=0)
        q = jnp.where(v_ok, q, 0.0)
        band_ref[...] = q[:, :TILE].T[:rows, :]
        for j in range(LAGS):
            d = half - j
            w = band_ref[2 * j:2 * j + 1, :]
            out = pltpu.roll(w, d % width, 1)
            out = jnp.where((x_i - d >= 0) & (x_i - d < width), out, 0.0)
            o_ref[0, 0, c, pl.ds(half + d, 1), :] = out[:, :TILE]
            o_ref[0, 1, c, pl.ds(half + d, 1), :] = out[:, TILE:]
        return carry

    lax.fori_loop(0, cb, one_channel, 0)


def lag_images(pair):
    n_src, _, shots, chans, t16, width = pair.shape
    cb = min(CB, chans)
    return pl.pallas_call(
        lag_kernel,
        grid=(shots, chans // cb),
        in_specs=[pl.BlockSpec((n_src, 2, 1, cb, t16, width), lambda i, j: (0, 0, i, j, 0, 0))],
        out_specs=pl.BlockSpec((1, 2, cb, LAGS, TILE), lambda i, j: (i, 0, j, 0, 0)),
        out_shape=jax.ShapeDtypeStruct((shots, 2, chans, LAGS, TILE), jnp.float32),
        scratch_shapes=[pltpu.VMEM((72, width), jnp.float32)],
    )(pair)


def place_tiles(image, first, base, slots):
    shots = image.shape[0]
    target = first[:, None] + jnp.arange(2, dtype=jnp.int32)[None, :] - base
    out = []
    for k in range(slots):
        acc = None
        for s in range(shots):
            for a in range(2):
                term = jnp.where(target[s, a] == k, image[s, a], 0.0)
                acc = term if acc is None else acc + term
        out.append(acc)
    return out


def flipped(x):
    width = x.shape[-1]
    i = jnp.arange(width, dtype=jnp.int32)
    anti = (i[:, None] + i[None, :] == width - 1).astype(x.dtype)
    return jnp.dot(x, anti, preferred_element_type=jnp.float32).astype(x.dtype)


def body(source_snap, receiver_snap, start_tile):
    owner = lax.axis_index("space")
    receiver_snap = flipped(receiver_snap)
    images = []
    received = []
    first = 0
    for g, size in enumerate(CHUNKS):
        cs = slice(first, first + size)
        first += size
        pair = jnp.stack([source_snap[:, :, cs], receiver_snap[:, :, cs]])
        pair = jnp.transpose(pair, (4, 0, 1, 3, 2, 5))
        if g >= 1:
            pair, received[g - 1] = lax.optimization_barrier((pair, received[g - 1]))
        if g >= 2:
            pair, images[g - 2] = lax.optimization_barrier((pair, images[g - 2]))
        received.append(lax.all_to_all(pair, "tm", split_axis=0, concat_axis=0, tiled=True))
        if g >= 1:
            images.append(lag_images(received[g - 1]))
    images.append(lag_images(received[-1]))
    placed = [place_tiles(image, start_tile, owner - 1, 3) for image in images]
    slots = [jnp.concatenate([p[k] for p in placed], axis=0) for k in range(3)]
    right_part = passed_along(slots[0], "space", -1)
    left_part = passed_along(slots[2], "space", 1)
    return (slots[1] + right_part + left_part)[None]


def solution(mesh):
    in_specs = (P("space", "tm", None, None, None), P("space", "tm", None, None, None), P("space"))
    out_specs = P("tm", None, None, "space")
    return jax.shard_map(body, mesh=mesh, in_specs=in_specs, out_specs=out_specs, check_vma=False)
```

```python
import functools

import jax
import jax.numpy as jnp
from jax import lax
from jax.experimental import pallas as pl
from jax.experimental.pallas import tpu as pltpu
from jax.sharding import PartitionSpec as P

LAGS = 33
TILE = 128
CB = 8
CHUNKS = (48, 16)


def passed_along(block, axis, distance):
    devices = range(lax.axis_size(axis))
    route = [(i - distance, i) for i in devices if i - distance in devices]
    return lax.ppermute(block, axis, route)


def lag_kernel(x_ref, o_ref, band_ref):
    src, _, _, cb, t16, width = x_ref.shape
    half = (LAGS - 1) // 2
    rows = band_ref.shape[0]
    u_i = lax.broadcasted_iota(jnp.int32, (width, width), 0)
    k_i = lax.broadcasted_iota(jnp.int32, (width, width), 1)
    v_ok = (u_i - k_i + 2 * half >= 0) & (u_i - k_i + 2 * half < width)
    x_i = lax.broadcasted_iota(jnp.int32, (1, width), 1)
    a_i = lax.broadcasted_iota(jnp.int32, (TILE, TILE), 0)
    b_i = lax.broadcasted_iota(jnp.int32, (TILE, TILE), 1)
    anti = jnp.where(a_i + b_i == TILE - 1, 1.0, 0.0).astype(jnp.bfloat16)

    def one_channel(c, carry):
        s_t = x_ref[:, 0, 0, c, :, :].reshape(src * t16, width)
        r_t = x_ref[:, 1, 0, c, :, :].reshape(src * t16, width)
        swapped = jnp.concatenate([r_t[:, TILE:], r_t[:, :TILE]], axis=0)
        rev = jnp.dot(swapped, anti, preferred_element_type=jnp.float32).astype(jnp.bfloat16)
        r_t = jnp.concatenate([rev[:src * t16], rev[src * t16:]], axis=1)
        g = lax.dot_general(s_t, r_t, (((0,), (0,)), ((), ())),
                            preferred_element_type=jnp.float32)
        q = pltpu.roll(g, 2 * half + 1, 1, stride=1, stride_axis=0)
        q = jnp.where(v_ok, q, 0.0)
        band_ref[...] = q[:, :TILE].T[:rows, :]
        for j in range(LAGS):
            d = half - j
            w = band_ref[2 * j:2 * j + 1, :]
            out = pltpu.roll(w, d % width, 1)
            out = jnp.where((x_i - d >= 0) & (x_i - d < width), out, 0.0)
            o_ref[0, 0, c, pl.ds(half + d, 1), :] = out[:, :TILE]
            o_ref[0, 1, c, pl.ds(half + d, 1), :] = out[:, TILE:]
        return carry

    lax.fori_loop(0, cb, one_channel, 0)


def lag_images(pair):
    n_src, _, shots, chans, t16, width = pair.shape
    cb = min(CB, chans)
    return pl.pallas_call(
        lag_kernel,
        grid=(shots, chans // cb),
        in_specs=[pl.BlockSpec((n_src, 2, 1, cb, t16, width), lambda i, j: (0, 0, i, j, 0, 0))],
        out_specs=pl.BlockSpec((1, 2, cb, LAGS, TILE), lambda i, j: (i, 0, j, 0, 0)),
        out_shape=jax.ShapeDtypeStruct((shots, 2, chans, LAGS, TILE), jnp.float32),
        scratch_shapes=[pltpu.VMEM((72, width), jnp.float32)],
    )(pair)


def place_tiles(image, first, base, slots):
    shots = image.shape[0]
    target = first[:, None] + jnp.arange(2, dtype=jnp.int32)[None, :] - base
    out = []
    for k in range(slots):
        acc = None
        for s in range(shots):
            for a in range(2):
                term = jnp.where(target[s, a] == k, image[s, a], 0.0)
                acc = term if acc is None else acc + term
        out.append(acc)
    return out


def flipped(x):
    width = x.shape[-1]
    i = jnp.arange(width, dtype=jnp.int32)
    anti = (i[:, None] + i[None, :] == width - 1).astype(x.dtype)
    return jnp.dot(x, anti, preferred_element_type=jnp.float32).astype(x.dtype)


def body(source_snap, receiver_snap, start_tile):
    owner = lax.axis_index("space")
    images = []
    received = []
    first = 0
    for g, size in enumerate(CHUNKS):
        cs = slice(first, first + size)
        first += size
        pair = jnp.stack([source_snap[:, :, cs], receiver_snap[:, :, cs]])
        pair = jnp.transpose(pair, (4, 0, 1, 3, 2, 5))
        if g >= 1:
            pair, received[g - 1] = lax.optimization_barrier((pair, received[g - 1]))
        if g >= 2:
            pair, images[g - 2] = lax.optimization_barrier((pair, images[g - 2]))
        received.append(lax.all_to_all(pair, "tm", split_axis=0, concat_axis=0, tiled=True))
        if g >= 1:
            images.append(lag_images(received[g - 1]))
    images.append(lag_images(received[-1]))
    placed = [place_tiles(image, start_tile, owner - 1, 3) for image in images]
    slots = [jnp.concatenate([p[k] for p in placed], axis=0) for k in range(3)]
    right_part = passed_along(slots[0], "space", -1)
    left_part = passed_along(slots[2], "space", 1)
    return (slots[1] + right_part + left_part)[None]


def solution(mesh):
    in_specs = (P("space", "tm", None, None, None), P("space", "tm", None, None, None), P("space"))
    out_specs = P("tm", None, None, "space")
    return jax.shard_map(body, mesh=mesh, in_specs=in_specs, out_specs=out_specs, check_vma=False)
```

```python
import functools

import jax
import jax.numpy as jnp
from jax import lax
from jax.experimental import pallas as pl
from jax.experimental.pallas import tpu as pltpu
from jax.sharding import PartitionSpec as P

LAGS = 33
TILE = 128
CB = 8
CHUNKS = (48, 16)


def passed_along(block, axis, distance):
    devices = range(lax.axis_size(axis))
    route = [(i - distance, i) for i in devices if i - distance in devices]
    return lax.ppermute(block, axis, route)


def lag_kernel(x_ref, o_ref, band_ref):
    src, _, _, cb, t16, width = x_ref.shape
    half = (LAGS - 1) // 2
    rows = band_ref.shape[0]
    u_i = lax.broadcasted_iota(jnp.int32, (width, width), 0)
    k_i = lax.broadcasted_iota(jnp.int32, (width, width), 1)
    v_ok = (u_i - k_i + 2 * half >= 0) & (u_i - k_i + 2 * half < width)
    x_i = lax.broadcasted_iota(jnp.int32, (1, width), 1)
    a_i = lax.broadcasted_iota(jnp.int32, (TILE, TILE), 0)
    b_i = lax.broadcasted_iota(jnp.int32, (TILE, TILE), 1)
    anti = jnp.where(a_i + b_i == TILE - 1, 1.0, 0.0).astype(jnp.bfloat16)

    def one_channel(c, carry):
        s_t = x_ref[:, 0, 0, c, :, :].reshape(src * t16, width)
        r_t = x_ref[:, 1, 0, c, :, :].reshape(src * t16, width)
        swapped = jnp.concatenate([r_t[:, TILE:], r_t[:, :TILE]], axis=0)
        rev = jnp.dot(swapped, anti, preferred_element_type=jnp.float32).astype(jnp.bfloat16)
        r_t = jnp.concatenate([rev[:src * t16], rev[src * t16:]], axis=1)
        g = lax.dot_general(s_t, r_t, (((0,), (0,)), ((), ())),
                            preferred_element_type=jnp.float32)
        q = pltpu.roll(g, 2 * half + 1, 1, stride=1, stride_axis=0)
        q = jnp.where(v_ok, q, 0.0)
        band_ref[...] = q[:, :TILE].T[:rows, :]
        for j in range(LAGS):
            d = half - j
            w = band_ref[2 * j:2 * j + 1, :]
            out = pltpu.roll(w, d % width, 1)
            out = jnp.where((x_i - d >= 0) & (x_i - d < width), out, 0.0)
            o_ref[0, 0, c, pl.ds(half + d, 1), :] = out[:, :TILE]
            o_ref[0, 1, c, pl.ds(half + d, 1), :] = out[:, TILE:]
        return carry

    lax.fori_loop(0, cb, one_channel, 0)


def lag_images(pair):
    n_src, _, shots, chans, t16, width = pair.shape
    cb = min(CB, chans)
    return pl.pallas_call(
        lag_kernel,
        grid=(shots, chans // cb),
        in_specs=[pl.BlockSpec((n_src, 2, 1, cb, t16, width), lambda i, j: (0, 0, i, j, 0, 0))],
        out_specs=pl.BlockSpec((1, 2, cb, LAGS, TILE), lambda i, j: (i, 0, j, 0, 0)),
        out_shape=jax.ShapeDtypeStruct((shots, 2, chans, LAGS, TILE), jnp.float32),
        scratch_shapes=[pltpu.VMEM((72, width), jnp.float32)],
    )(pair)


def place_tiles(image, first, base, slots):
    shots = image.shape[0]
    target = first[:, None] + jnp.arange(2, dtype=jnp.int32)[None, :] - base
    out = []
    for k in range(slots):
        acc = None
        for s in range(shots):
            for a in range(2):
                term = jnp.where(target[s, a] == k, image[s, a], 0.0)
                acc = term if acc is None else acc + term
        out.append(acc)
    return out


def flipped(x):
    width = x.shape[-1]
    i = jnp.arange(width, dtype=jnp.int32)
    anti = (i[:, None] + i[None, :] == width - 1).astype(x.dtype)
    return jnp.dot(x, anti, preferred_element_type=jnp.float32).astype(x.dtype)


def exchanged(pair):
    n = lax.axis_size("tm")
    j = lax.axis_index("tm")
    pieces = []
    for o in range(n):
        piece = lax.dynamic_slice_in_dim(pair, (j + o) % n, 1, axis=0)
        if o:
            piece = lax.ppermute(piece, "tm", [(i, (i + o) % n) for i in range(n)])
        pieces.append(piece)
    return jnp.concatenate(pieces, axis=0)


def body(source_snap, receiver_snap, start_tile):
    owner = lax.axis_index("space")
    images = []
    received = []
    first = 0
    for g, size in enumerate(CHUNKS):
        cs = slice(first, first + size)
        first += size
        pair = jnp.stack([source_snap[:, :, cs], receiver_snap[:, :, cs]])
        pair = jnp.transpose(pair, (4, 0, 1, 3, 2, 5))
        if g >= 1:
            pair, received[g - 1] = lax.optimization_barrier((pair, received[g - 1]))
        if g >= 2:
            pair, images[g - 2] = lax.optimization_barrier((pair, images[g - 2]))
        received.append(exchanged(pair))
        if g >= 1:
            images.append(lag_images(received[g - 1]))
    images.append(lag_images(received[-1]))
    placed = [place_tiles(image, start_tile, owner - 1, 3) for image in images]
    slots = [jnp.concatenate([p[k] for p in placed], axis=0) for k in range(3)]
    right_part = passed_along(slots[0], "space", -1)
    left_part = passed_along(slots[2], "space", 1)
    return (slots[1] + right_part + left_part)[None]


def solution(mesh):
    in_specs = (P("space", "tm", None, None, None), P("space", "tm", None, None, None), P("space"))
    out_specs = P("tm", None, None, "space")
    return jax.shard_map(body, mesh=mesh, in_specs=in_specs, out_specs=out_specs, check_vma=False)
```

```python
import functools

import jax
import jax.numpy as jnp
from jax import lax
from jax.experimental import pallas as pl
from jax.experimental.pallas import tpu as pltpu
from jax.sharding import PartitionSpec as P

LAGS = 33
TILE = 128
CB = 8
CHUNKS = (32, 24, 8)


def passed_along(block, axis, distance):
    devices = range(lax.axis_size(axis))
    route = [(i - distance, i) for i in devices if i - distance in devices]
    return lax.ppermute(block, axis, route)


def lag_kernel(x_ref, o_ref, band_ref):
    src, _, _, cb, t16, width = x_ref.shape
    half = (LAGS - 1) // 2
    rows = band_ref.shape[0]
    u_i = lax.broadcasted_iota(jnp.int32, (width, width), 0)
    k_i = lax.broadcasted_iota(jnp.int32, (width, width), 1)
    v_ok = (u_i - k_i + 2 * half >= 0) & (u_i - k_i + 2 * half < width)
    x_i = lax.broadcasted_iota(jnp.int32, (1, width), 1)
    a_i = lax.broadcasted_iota(jnp.int32, (TILE, TILE), 0)
    b_i = lax.broadcasted_iota(jnp.int32, (TILE, TILE), 1)
    anti = jnp.where(a_i + b_i == TILE - 1, 1.0, 0.0).astype(jnp.bfloat16)

    def one_channel(c, carry):
        s_t = x_ref[:, 0, 0, c, :, :].reshape(src * t16, width)
        r_t = x_ref[:, 1, 0, c, :, :].reshape(src * t16, width)
        swapped = jnp.concatenate([r_t[:, TILE:], r_t[:, :TILE]], axis=0)
        rev = jnp.dot(swapped, anti, preferred_element_type=jnp.float32).astype(jnp.bfloat16)
        r_t = jnp.concatenate([rev[:src * t16], rev[src * t16:]], axis=1)
        g = lax.dot_general(s_t, r_t, (((0,), (0,)), ((), ())),
                            preferred_element_type=jnp.float32)
        q = pltpu.roll(g, 2 * half + 1, 1, stride=1, stride_axis=0)
        q = jnp.where(v_ok, q, 0.0)
        band_ref[...] = q[:, :TILE].T[:rows, :]
        for j in range(LAGS):
            d = half - j
            w = band_ref[2 * j:2 * j + 1, :]
            out = pltpu.roll(w, d % width, 1)
            out = jnp.where((x_i - d >= 0) & (x_i - d < width), out, 0.0)
            o_ref[0, 0, c, pl.ds(half + d, 1), :] = out[:, :TILE]
            o_ref[0, 1, c, pl.ds(half + d, 1), :] = out[:, TILE:]
        return carry

    lax.fori_loop(0, cb, one_channel, 0)


def lag_images(pair):
    n_src, _, shots, chans, t16, width = pair.shape
    cb = min(CB, chans)
    return pl.pallas_call(
        lag_kernel,
        grid=(shots, chans // cb),
        in_specs=[pl.BlockSpec((n_src, 2, 1, cb, t16, width), lambda i, j: (0, 0, i, j, 0, 0))],
        out_specs=pl.BlockSpec((1, 2, cb, LAGS, TILE), lambda i, j: (i, 0, j, 0, 0)),
        out_shape=jax.ShapeDtypeStruct((shots, 2, chans, LAGS, TILE), jnp.float32),
        scratch_shapes=[pltpu.VMEM((72, width), jnp.float32)],
    )(pair)


def place_tiles(image, first, base, slots):
    shots = image.shape[0]
    target = first[:, None] + jnp.arange(2, dtype=jnp.int32)[None, :] - base
    out = []
    for k in range(slots):
        acc = None
        for s in range(shots):
            for a in range(2):
                term = jnp.where(target[s, a] == k, image[s, a], 0.0)
                acc = term if acc is None else acc + term
        out.append(acc)
    return out


def flipped(x):
    width = x.shape[-1]
    i = jnp.arange(width, dtype=jnp.int32)
    anti = (i[:, None] + i[None, :] == width - 1).astype(x.dtype)
    return jnp.dot(x, anti, preferred_element_type=jnp.float32).astype(x.dtype)


def body(source_snap, receiver_snap, start_tile):
    owner = lax.axis_index("space")
    images = []
    received = []
    first = 0
    for g, size in enumerate(CHUNKS):
        cs = slice(first, first + size)
        first += size
        pair = jnp.stack([source_snap[:, :, cs], receiver_snap[:, :, cs]])
        pair = jnp.transpose(pair, (4, 0, 1, 3, 2, 5))
        if g >= 1:
            pair, received[g - 1] = lax.optimization_barrier((pair, received[g - 1]))
        if g >= 2:
            pair, images[g - 2] = lax.optimization_barrier((pair, images[g - 2]))
        received.append(lax.all_to_all(pair, "tm", split_axis=0, concat_axis=0, tiled=True))
        if g >= 1:
            images.append(lag_images(received[g - 1]))
    images.append(lag_images(received[-1]))
    placed = [place_tiles(image, start_tile, owner - 1, 3) for image in images]
    slots = [jnp.concatenate([p[k] for p in placed], axis=0) for k in range(3)]
    right_part = passed_along(slots[0], "space", -1)
    left_part = passed_along(slots[2], "space", 1)
    return (slots[1] + right_part + left_part)[None]


def solution(mesh):
    in_specs = (P("space", "tm", None, None, None), P("space", "tm", None, None, None), P("space"))
    out_specs = P("tm", None, None, "space")
    return jax.shard_map(body, mesh=mesh, in_specs=in_specs, out_specs=out_specs, check_vma=False)
```

```python
import functools

import jax
import jax.numpy as jnp
from jax import lax
from jax.experimental import pallas as pl
from jax.experimental.pallas import tpu as pltpu
from jax.sharding import PartitionSpec as P

LAGS = 33
TILE = 128
CB = 8
CHUNKS = (32, 24, 8)


def passed_along(block, axis, distance):
    devices = range(lax.axis_size(axis))
    route = [(i - distance, i) for i in devices if i - distance in devices]
    return lax.ppermute(block, axis, route)


def lag_kernel(x_ref, o_ref, band_ref):
    src, _, _, cb, t16, width = x_ref.shape
    half = (LAGS - 1) // 2
    rows = band_ref.shape[0]
    u_i = lax.broadcasted_iota(jnp.int32, (width, width), 0)
    k_i = lax.broadcasted_iota(jnp.int32, (width, width), 1)
    v_ok = (u_i - k_i + 2 * half >= 0) & (u_i - k_i + 2 * half < width)
    x_i = lax.broadcasted_iota(jnp.int32, (1, width), 1)
    a_i = lax.broadcasted_iota(jnp.int32, (TILE, TILE), 0)
    b_i = lax.broadcasted_iota(jnp.int32, (TILE, TILE), 1)
    anti = jnp.where(a_i + b_i == TILE - 1, 1.0, 0.0).astype(jnp.bfloat16)

    def one_channel(c, carry):
        s_t = x_ref[:, 0, 0, c, :, :].reshape(src * t16, width)
        r_t = x_ref[:, 1, 0, c, :, :].reshape(src * t16, width)
        swapped = jnp.concatenate([r_t[:, TILE:], r_t[:, :TILE]], axis=0)
        rev = jnp.dot(swapped, anti, preferred_element_type=jnp.float32).astype(jnp.bfloat16)
        r_t = jnp.concatenate([rev[:src * t16], rev[src * t16:]], axis=1)
        g = lax.dot_general(s_t, r_t, (((0,), (0,)), ((), ())),
                            preferred_element_type=jnp.float32)
        q = pltpu.roll(g, 2 * half + 1, 1, stride=1, stride_axis=0)
        q = jnp.where(v_ok, q, 0.0)
        band_ref[...] = q[:, :TILE].T[:rows, :]
        for j in range(LAGS):
            d = half - j
            w = band_ref[2 * j:2 * j + 1, :]
            out = pltpu.roll(w, d % width, 1)
            out = jnp.where((x_i - d >= 0) & (x_i - d < width), out, 0.0)
            o_ref[0, 0, c, pl.ds(half + d, 1), :] = out[:, :TILE]
            o_ref[0, 1, c, pl.ds(half + d, 1), :] = out[:, TILE:]
        return carry

    lax.fori_loop(0, cb, one_channel, 0, unroll=2)


def lag_images(pair):
    n_src, _, shots, chans, t16, width = pair.shape
    cb = min(CB, chans)
    return pl.pallas_call(
        lag_kernel,
        grid=(shots, chans // cb),
        in_specs=[pl.BlockSpec((n_src, 2, 1, cb, t16, width), lambda i, j: (0, 0, i, j, 0, 0))],
        out_specs=pl.BlockSpec((1, 2, cb, LAGS, TILE), lambda i, j: (i, 0, j, 0, 0)),
        out_shape=jax.ShapeDtypeStruct((shots, 2, chans, LAGS, TILE), jnp.float32),
        scratch_shapes=[pltpu.VMEM((72, width), jnp.float32)],
    )(pair)


def place_tiles(image, first, base, slots):
    shots = image.shape[0]
    target = first[:, None] + jnp.arange(2, dtype=jnp.int32)[None, :] - base
    out = []
    for k in range(slots):
        acc = None
        for s in range(shots):
            for a in range(2):
                term = jnp.where(target[s, a] == k, image[s, a], 0.0)
                acc = term if acc is None else acc + term
        out.append(acc)
    return out


def flipped(x):
    width = x.shape[-1]
    i = jnp.arange(width, dtype=jnp.int32)
    anti = (i[:, None] + i[None, :] == width - 1).astype(x.dtype)
    return jnp.dot(x, anti, preferred_element_type=jnp.float32).astype(x.dtype)


def body(source_snap, receiver_snap, start_tile):
    owner = lax.axis_index("space")
    images = []
    received = []
    first = 0
    for g, size in enumerate(CHUNKS):
        cs = slice(first, first + size)
        first += size
        pair = jnp.stack([source_snap[:, :, cs], receiver_snap[:, :, cs]])
        pair = jnp.transpose(pair, (4, 0, 1, 3, 2, 5))
        if g >= 1:
            pair, received[g - 1] = lax.optimization_barrier((pair, received[g - 1]))
        if g >= 2:
            pair, images[g - 2] = lax.optimization_barrier((pair, images[g - 2]))
        received.append(lax.all_to_all(pair, "tm", split_axis=0, concat_axis=0, tiled=True))
        if g >= 1:
            images.append(lag_images(received[g - 1]))
    images.append(lag_images(received[-1]))
    placed = [place_tiles(image, start_tile, owner - 1, 3) for image in images]
    slots = [jnp.concatenate([p[k] for p in placed], axis=0) for k in range(3)]
    right_part = passed_along(slots[0], "space", -1)
    left_part = passed_along(slots[2], "space", 1)
    return (slots[1] + right_part + left_part)[None]


def solution(mesh):
    in_specs = (P("space", "tm", None, None, None), P("space", "tm", None, None, None), P("space"))
    out_specs = P("tm", None, None, "space")
    return jax.shard_map(body, mesh=mesh, in_specs=in_specs, out_specs=out_specs, check_vma=False)
```

```python
import functools

import jax
import jax.numpy as jnp
from jax import lax
from jax.experimental import pallas as pl
from jax.experimental.pallas import tpu as pltpu
from jax.sharding import PartitionSpec as P

LAGS = 33
TILE = 128
CB = 8
CHUNKS = (32, 24, 8)


def passed_along(block, axis, distance):
    devices = range(lax.axis_size(axis))
    route = [(i - distance, i) for i in devices if i - distance in devices]
    return lax.ppermute(block, axis, route)


def lag_kernel(x_ref, o_ref, band_ref):
    src, _, _, cb, t16, width = x_ref.shape
    half = (LAGS - 1) // 2
    rows = band_ref.shape[0]
    u_i = lax.broadcasted_iota(jnp.int32, (width, width), 0)
    k_i = lax.broadcasted_iota(jnp.int32, (width, width), 1)
    v_ok = (u_i - k_i + 2 * half >= 0) & (u_i - k_i + 2 * half < width)
    x_i = lax.broadcasted_iota(jnp.int32, (1, width), 1)
    a_i = lax.broadcasted_iota(jnp.int32, (TILE, TILE), 0)
    b_i = lax.broadcasted_iota(jnp.int32, (TILE, TILE), 1)
    anti = jnp.where(a_i + b_i == TILE - 1, 1.0, 0.0).astype(jnp.bfloat16)

    def one_channel(c, carry):
        s_t = x_ref[:, 0, 0, c, :, :].reshape(src * t16, width)
        r_t = x_ref[:, 1, 0, c, :, :].reshape(src * t16, width)
        swapped = jnp.concatenate([r_t[:, TILE:], r_t[:, :TILE]], axis=0)
        rev = jnp.dot(swapped, anti, preferred_element_type=jnp.float32).astype(jnp.bfloat16)
        r_t = jnp.concatenate([rev[:src * t16], rev[src * t16:]], axis=1)
        g = lax.dot_general(s_t, r_t, (((0,), (0,)), ((), ())),
                            preferred_element_type=jnp.float32)
        q = pltpu.roll(g, 2 * half + 1, 1, stride=1, stride_axis=0)
        q = jnp.where(v_ok, q, 0.0)
        band_ref[...] = q[:, :TILE].T[:rows, :]
        for j in range(LAGS):
            d = half - j
            w = band_ref[2 * j:2 * j + 1, :]
            out = pltpu.roll(w, d % width, 1)
            out = jnp.where((x_i - d >= 0) & (x_i - d < width), out, 0.0)
            o_ref[0, 0, c, pl.ds(half + d, 1), :] = out[:, :TILE]
            o_ref[0, 1, c, pl.ds(half + d, 1), :] = out[:, TILE:]
        return carry

    lax.fori_loop(0, cb, one_channel, 0, unroll=4)


def lag_images(pair):
    n_src, _, shots, chans, t16, width = pair.shape
    cb = min(CB, chans)
    return pl.pallas_call(
        lag_kernel,
        grid=(shots, chans // cb),
        in_specs=[pl.BlockSpec((n_src, 2, 1, cb, t16, width), lambda i, j: (0, 0, i, j, 0, 0))],
        out_specs=pl.BlockSpec((1, 2, cb, LAGS, TILE), lambda i, j: (i, 0, j, 0, 0)),
        out_shape=jax.ShapeDtypeStruct((shots, 2, chans, LAGS, TILE), jnp.float32),
        scratch_shapes=[pltpu.VMEM((72, width), jnp.float32)],
    )(pair)


def place_tiles(image, first, base, slots):
    shots = image.shape[0]
    target = first[:, None] + jnp.arange(2, dtype=jnp.int32)[None, :] - base
    out = []
    for k in range(slots):
        acc = None
        for s in range(shots):
            for a in range(2):
                term = jnp.where(target[s, a] == k, image[s, a], 0.0)
                acc = term if acc is None else acc + term
        out.append(acc)
    return out


def flipped(x):
    width = x.shape[-1]
    i = jnp.arange(width, dtype=jnp.int32)
    anti = (i[:, None] + i[None, :] == width - 1).astype(x.dtype)
    return jnp.dot(x, anti, preferred_element_type=jnp.float32).astype(x.dtype)


def body(source_snap, receiver_snap, start_tile):
    owner = lax.axis_index("space")
    images = []
    received = []
    first = 0
    for g, size in enumerate(CHUNKS):
        cs = slice(first, first + size)
        first += size
        pair = jnp.stack([source_snap[:, :, cs], receiver_snap[:, :, cs]])
        pair = jnp.transpose(pair, (4, 0, 1, 3, 2, 5))
        if g >= 1:
            pair, received[g - 1] = lax.optimization_barrier((pair, received[g - 1]))
        if g >= 2:
            pair, images[g - 2] = lax.optimization_barrier((pair, images[g - 2]))
        received.append(lax.all_to_all(pair, "tm", split_axis=0, concat_axis=0, tiled=True))
        if g >= 1:
            images.append(lag_images(received[g - 1]))
    images.append(lag_images(received[-1]))
    placed = [place_tiles(image, start_tile, owner - 1, 3) for image in images]
    slots = [jnp.concatenate([p[k] for p in placed], axis=0) for k in range(3)]
    right_part = passed_along(slots[0], "space", -1)
    left_part = passed_along(slots[2], "space", 1)
    return (slots[1] + right_part + left_part)[None]


def solution(mesh):
    in_specs = (P("space", "tm", None, None, None), P("space", "tm", None, None, None), P("space"))
    out_specs = P("tm", None, None, "space")
    return jax.shard_map(body, mesh=mesh, in_specs=in_specs, out_specs=out_specs, check_vma=False)
```

```python
import functools

import jax
import jax.numpy as jnp
from jax import lax
from jax.experimental import pallas as pl
from jax.experimental.pallas import tpu as pltpu
from jax.sharding import PartitionSpec as P

LAGS = 33
TILE = 128
CB = 8
CHUNKS = (8, 40, 16)


def passed_along(block, axis, distance):
    devices = range(lax.axis_size(axis))
    route = [(i - distance, i) for i in devices if i - distance in devices]
    return lax.ppermute(block, axis, route)


def lag_kernel(x_ref, o_ref, band_ref):
    src, _, _, cb, t16, width = x_ref.shape
    half = (LAGS - 1) // 2
    rows = band_ref.shape[0]
    u_i = lax.broadcasted_iota(jnp.int32, (width, width), 0)
    k_i = lax.broadcasted_iota(jnp.int32, (width, width), 1)
    v_ok = (u_i - k_i + 2 * half >= 0) & (u_i - k_i + 2 * half < width)
    x_i = lax.broadcasted_iota(jnp.int32, (1, width), 1)
    a_i = lax.broadcasted_iota(jnp.int32, (TILE, TILE), 0)
    b_i = lax.broadcasted_iota(jnp.int32, (TILE, TILE), 1)
    anti = jnp.where(a_i + b_i == TILE - 1, 1.0, 0.0).astype(jnp.bfloat16)

    def one_channel(c, carry):
        s_t = x_ref[:, 0, 0, c, :, :].reshape(src * t16, width)
        r_t = x_ref[:, 1, 0, c, :, :].reshape(src * t16, width)
        swapped = jnp.concatenate([r_t[:, TILE:], r_t[:, :TILE]], axis=0)
        rev = jnp.dot(swapped, anti, preferred_element_type=jnp.float32).astype(jnp.bfloat16)
        r_t = jnp.concatenate([rev[:src * t16], rev[src * t16:]], axis=1)
        g = lax.dot_general(s_t, r_t, (((0,), (0,)), ((), ())),
                            preferred_element_type=jnp.float32)
        q = pltpu.roll(g, 2 * half + 1, 1, stride=1, stride_axis=0)
        q = jnp.where(v_ok, q, 0.0)
        band_ref[...] = q[:, :TILE].T[:rows, :]
        for j in range(LAGS):
            d = half - j
            w = band_ref[2 * j:2 * j + 1, :]
            out = pltpu.roll(w, d % width, 1)
            out = jnp.where((x_i - d >= 0) & (x_i - d < width), out, 0.0)
            o_ref[0, 0, c, pl.ds(half + d, 1), :] = out[:, :TILE]
            o_ref[0, 1, c, pl.ds(half + d, 1), :] = out[:, TILE:]
        return carry

    lax.fori_loop(0, cb, one_channel, 0, unroll=2)


def lag_images(pair):
    n_src, _, shots, chans, t16, width = pair.shape
    cb = min(CB, chans)
    return pl.pallas_call(
        lag_kernel,
        grid=(shots, chans // cb),
        in_specs=[pl.BlockSpec((n_src, 2, 1, cb, t16, width), lambda i, j: (0, 0, i, j, 0, 0))],
        out_specs=pl.BlockSpec((1, 2, cb, LAGS, TILE), lambda i, j: (i, 0, j, 0, 0)),
        out_shape=jax.ShapeDtypeStruct((shots, 2, chans, LAGS, TILE), jnp.float32),
        scratch_shapes=[pltpu.VMEM((72, width), jnp.float32)],
    )(pair)


def place_tiles(image, first, base, slots):
    shots = image.shape[0]
    target = first[:, None] + jnp.arange(2, dtype=jnp.int32)[None, :] - base
    out = []
    for k in range(slots):
        acc = None
        for s in range(shots):
            for a in range(2):
                term = jnp.where(target[s, a] == k, image[s, a], 0.0)
                acc = term if acc is None else acc + term
        out.append(acc)
    return out


def flipped(x):
    width = x.shape[-1]
    i = jnp.arange(width, dtype=jnp.int32)
    anti = (i[:, None] + i[None, :] == width - 1).astype(x.dtype)
    return jnp.dot(x, anti, preferred_element_type=jnp.float32).astype(x.dtype)


def body(source_snap, receiver_snap, start_tile):
    owner = lax.axis_index("space")
    images = []
    received = []
    first = 0
    for g, size in enumerate(CHUNKS):
        cs = slice(first, first + size)
        first += size
        pair = jnp.stack([source_snap[:, :, cs], receiver_snap[:, :, cs]])
        pair = jnp.transpose(pair, (4, 0, 1, 3, 2, 5))
        if g >= 1:
            pair, received[g - 1] = lax.optimization_barrier((pair, received[g - 1]))
        if g >= 2:
            pair, images[g - 2] = lax.optimization_barrier((pair, images[g - 2]))
        received.append(lax.all_to_all(pair, "tm", split_axis=0, concat_axis=0, tiled=True))
        if g >= 1:
            images.append(lag_images(received[g - 1]))
    images.append(lag_images(received[-1]))
    placed = [place_tiles(image, start_tile, owner - 1, 3) for image in images]
    slots = [jnp.concatenate([p[k] for p in placed], axis=0) for k in range(3)]
    right_part = passed_along(slots[0], "space", -1)
    left_part = passed_along(slots[2], "space", 1)
    return (slots[1] + right_part + left_part)[None]


def solution(mesh):
    in_specs = (P("space", "tm", None, None, None), P("space", "tm", None, None, None), P("space"))
    out_specs = P("tm", None, None, "space")
    return jax.shard_map(body, mesh=mesh, in_specs=in_specs, out_specs=out_specs, check_vma=False)
```

```python
import functools

import jax
import jax.numpy as jnp
from jax import lax
from jax.experimental import pallas as pl
from jax.experimental.pallas import tpu as pltpu
from jax.sharding import PartitionSpec as P

LAGS = 33
TILE = 128
CB = 8
CHUNKS = (8, 48, 8)


def passed_along(block, axis, distance):
    devices = range(lax.axis_size(axis))
    route = [(i - distance, i) for i in devices if i - distance in devices]
    return lax.ppermute(block, axis, route)


def lag_kernel(x_ref, o_ref, band_ref):
    src, _, _, cb, t16, width = x_ref.shape
    half = (LAGS - 1) // 2
    rows = band_ref.shape[0]
    u_i = lax.broadcasted_iota(jnp.int32, (width, width), 0)
    k_i = lax.broadcasted_iota(jnp.int32, (width, width), 1)
    v_ok = (u_i - k_i + 2 * half >= 0) & (u_i - k_i + 2 * half < width)
    x_i = lax.broadcasted_iota(jnp.int32, (1, width), 1)
    a_i = lax.broadcasted_iota(jnp.int32, (TILE, TILE), 0)
    b_i = lax.broadcasted_iota(jnp.int32, (TILE, TILE), 1)
    anti = jnp.where(a_i + b_i == TILE - 1, 1.0, 0.0).astype(jnp.bfloat16)

    def one_channel(c, carry):
        s_t = x_ref[:, 0, 0, c, :, :].reshape(src * t16, width)
        r_t = x_ref[:, 1, 0, c, :, :].reshape(src * t16, width)
        swapped = jnp.concatenate([r_t[:, TILE:], r_t[:, :TILE]], axis=0)
        rev = jnp.dot(swapped, anti, preferred_element_type=jnp.float32).astype(jnp.bfloat16)
        r_t = jnp.concatenate([rev[:src * t16], rev[src * t16:]], axis=1)
        g = lax.dot_general(s_t, r_t, (((0,), (0,)), ((), ())),
                            preferred_element_type=jnp.float32)
        q = pltpu.roll(g, 2 * half + 1, 1, stride=1, stride_axis=0)
        q = jnp.where(v_ok, q, 0.0)
        band_ref[...] = q[:, :TILE].T[:rows, :]
        for j in range(LAGS):
            d = half - j
            w = band_ref[2 * j:2 * j + 1, :]
            out = pltpu.roll(w, d % width, 1)
            out = jnp.where((x_i - d >= 0) & (x_i - d < width), out, 0.0)
            o_ref[0, 0, c, pl.ds(half + d, 1), :] = out[:, :TILE]
            o_ref[0, 1, c, pl.ds(half + d, 1), :] = out[:, TILE:]
        return carry

    lax.fori_loop(0, cb, one_channel, 0, unroll=2)


def lag_images(pair):
    n_src, _, shots, chans, t16, width = pair.shape
    cb = min(CB, chans)
    return pl.pallas_call(
        lag_kernel,
        grid=(shots, chans // cb),
        in_specs=[pl.BlockSpec((n_src, 2, 1, cb, t16, width), lambda i, j: (0, 0, i, j, 0, 0))],
        out_specs=pl.BlockSpec((1, 2, cb, LAGS, TILE), lambda i, j: (i, 0, j, 0, 0)),
        out_shape=jax.ShapeDtypeStruct((shots, 2, chans, LAGS, TILE), jnp.float32),
        scratch_shapes=[pltpu.VMEM((72, width), jnp.float32)],
    )(pair)


def place_tiles(image, first, base, slots):
    shots = image.shape[0]
    target = first[:, None] + jnp.arange(2, dtype=jnp.int32)[None, :] - base
    out = []
    for k in range(slots):
        acc = None
        for s in range(shots):
            for a in range(2):
                term = jnp.where(target[s, a] == k, image[s, a], 0.0)
                acc = term if acc is None else acc + term
        out.append(acc)
    return out


def flipped(x):
    width = x.shape[-1]
    i = jnp.arange(width, dtype=jnp.int32)
    anti = (i[:, None] + i[None, :] == width - 1).astype(x.dtype)
    return jnp.dot(x, anti, preferred_element_type=jnp.float32).astype(x.dtype)


def body(source_snap, receiver_snap, start_tile):
    owner = lax.axis_index("space")
    images = []
    received = []
    first = 0
    for g, size in enumerate(CHUNKS):
        cs = slice(first, first + size)
        first += size
        pair = jnp.stack([source_snap[:, :, cs], receiver_snap[:, :, cs]])
        pair = jnp.transpose(pair, (4, 0, 1, 3, 2, 5))
        if g >= 1:
            pair, received[g - 1] = lax.optimization_barrier((pair, received[g - 1]))
        if g >= 2:
            pair, images[g - 2] = lax.optimization_barrier((pair, images[g - 2]))
        received.append(lax.all_to_all(pair, "tm", split_axis=0, concat_axis=0, tiled=True))
        if g >= 1:
            images.append(lag_images(received[g - 1]))
    images.append(lag_images(received[-1]))
    placed = [place_tiles(image, start_tile, owner - 1, 3) for image in images]
    slots = [jnp.concatenate([p[k] for p in placed], axis=0) for k in range(3)]
    right_part = passed_along(slots[0], "space", -1)
    left_part = passed_along(slots[2], "space", 1)
    return (slots[1] + right_part + left_part)[None]


def solution(mesh):
    in_specs = (P("space", "tm", None, None, None), P("space", "tm", None, None, None), P("space"))
    out_specs = P("tm", None, None, "space")
    return jax.shard_map(body, mesh=mesh, in_specs=in_specs, out_specs=out_specs, check_vma=False)
```

```python
import functools

import jax
import jax.numpy as jnp
from jax import lax
from jax.experimental import pallas as pl
from jax.experimental.pallas import tpu as pltpu
from jax.sharding import PartitionSpec as P

LAGS = 33
TILE = 128
CB = 8
CHUNKS = (8, 40, 16)


def passed_along(block, axis, distance):
    devices = range(lax.axis_size(axis))
    route = [(i - distance, i) for i in devices if i - distance in devices]
    return lax.ppermute(block, axis, route)


def lag_kernel(x_ref, o_ref, band_ref):
    src, _, _, cb, t16, width = x_ref.shape
    half = (LAGS - 1) // 2
    rows = band_ref.shape[0]
    u_i = lax.broadcasted_iota(jnp.int32, (width, width), 0)
    k_i = lax.broadcasted_iota(jnp.int32, (width, width), 1)
    v_ok = (u_i - k_i + 2 * half >= 0) & (u_i - k_i + 2 * half < width)
    x_i = lax.broadcasted_iota(jnp.int32, (1, width), 1)
    a_i = lax.broadcasted_iota(jnp.int32, (TILE, TILE), 0)
    b_i = lax.broadcasted_iota(jnp.int32, (TILE, TILE), 1)
    anti = jnp.where(a_i + b_i == TILE - 1, 1.0, 0.0).astype(jnp.bfloat16)

    def one_channel(c, carry):
        s_t = x_ref[:, 0, 0, c, :, :].reshape(src * t16, width)
        r_t = x_ref[:, 1, 0, c, :, :].reshape(src * t16, width)
        swapped = jnp.concatenate([r_t[:, TILE:], r_t[:, :TILE]], axis=0)
        rev = jnp.dot(swapped, anti, preferred_element_type=jnp.float32).astype(jnp.bfloat16)
        r_t = jnp.concatenate([rev[:src * t16], rev[src * t16:]], axis=1)
        g = lax.dot_general(s_t, r_t, (((0,), (0,)), ((), ())),
                            preferred_element_type=jnp.float32)
        q = pltpu.roll(g, 2 * half + 1, 1, stride=1, stride_axis=0)
        q = jnp.where(v_ok, q, 0.0)
        band_ref[...] = q[:, :TILE].T[:rows, :]
        for j in range(LAGS):
            d = half - j
            w = band_ref[2 * j:2 * j + 1, :]
            out = pltpu.roll(w, d % width, 1)
            out = jnp.where((x_i - d >= 0) & (x_i - d < width), out, 0.0)
            o_ref[0, 0, c, pl.ds(half + d, 1), :] = out[:, :TILE]
            o_ref[0, 1, c, pl.ds(half + d, 1), :] = out[:, TILE:]
        return carry

    lax.fori_loop(0, cb, one_channel, 0, unroll=2)


def lag_images(pair):
    n_src, _, shots, chans, t16, width = pair.shape
    cb = min(CB, chans)
    return pl.pallas_call(
        lag_kernel,
        grid=(shots, chans // cb),
        in_specs=[pl.BlockSpec((n_src, 2, 1, cb, t16, width), lambda i, j: (0, 0, i, j, 0, 0))],
        out_specs=pl.BlockSpec((1, 2, cb, LAGS, TILE), lambda i, j: (i, 0, j, 0, 0)),
        out_shape=jax.ShapeDtypeStruct((shots, 2, chans, LAGS, TILE), jnp.float32),
        scratch_shapes=[pltpu.VMEM((72, width), jnp.float32)],
    )(pair)


def place_tiles(image, first, base, slots):
    shots = image.shape[0]
    target = first[:, None] + jnp.arange(2, dtype=jnp.int32)[None, :] - base
    out = []
    for k in range(slots):
        acc = None
        for s in range(shots):
            for a in range(2):
                term = jnp.where(target[s, a] == k, image[s, a], 0.0)
                acc = term if acc is None else acc + term
        out.append(acc)
    return out


def body(source_snap, receiver_snap, start_tile):
    owner = lax.axis_index("space")
    images = []
    received = []
    first = 0
    for g, size in enumerate(CHUNKS):
        cs = slice(first, first + size)
        first += size
        pair = jnp.stack([source_snap[:, :, cs], receiver_snap[:, :, cs]])
        pair = jnp.transpose(pair, (4, 0, 1, 3, 2, 5))
        if g >= 1:
            pair, received[g - 1] = lax.optimization_barrier((pair, received[g - 1]))
        if g >= 2:
            pair, images[g - 2] = lax.optimization_barrier((pair, images[g - 2]))
        received.append(lax.all_to_all(pair, "tm", split_axis=0, concat_axis=0, tiled=True))
        if g >= 1:
            images.append(lag_images(received[g - 1]))
    early = [place_tiles(image, start_tile, owner - 1, 3) for image in images]
    early = [jnp.concatenate([p[k] for p in early], axis=0) for k in range(3)]
    early, received[-1] = lax.optimization_barrier((early, received[-1]))
    parts = [early, place_tiles(lag_images(received[-1]), start_tile, owner - 1, 3)]
    out = []
    for slots in parts:
        right_part = passed_along(slots[0], "space", -1)
        left_part = passed_along(slots[2], "space", 1)
        out.append(slots[1] + right_part + left_part)
    return jnp.concatenate(out, axis=0)[None]


def solution(mesh):
    in_specs = (P("space", "tm", None, None, None), P("space", "tm", None, None, None), P("space"))
    out_specs = P("tm", None, None, "space")
    return jax.shard_map(body, mesh=mesh, in_specs=in_specs, out_specs=out_specs, check_vma=False)
```

```python
import functools

import jax
import jax.numpy as jnp
from jax import lax
from jax.experimental import pallas as pl
from jax.experimental.pallas import tpu as pltpu
from jax.sharding import PartitionSpec as P

LAGS = 33
TILE = 128
CB = 8
CHUNKS = (16, 40, 8)


def passed_along(block, axis, distance):
    devices = range(lax.axis_size(axis))
    route = [(i - distance, i) for i in devices if i - distance in devices]
    return lax.ppermute(block, axis, route)


def lag_kernel(x_ref, o_ref, band_ref):
    src, _, _, cb, t16, width = x_ref.shape
    half = (LAGS - 1) // 2
    rows = band_ref.shape[0]
    u_i = lax.broadcasted_iota(jnp.int32, (width, width), 0)
    k_i = lax.broadcasted_iota(jnp.int32, (width, width), 1)
    v_ok = (u_i - k_i + 2 * half >= 0) & (u_i - k_i + 2 * half < width)
    x_i = lax.broadcasted_iota(jnp.int32, (1, width), 1)
    a_i = lax.broadcasted_iota(jnp.int32, (TILE, TILE), 0)
    b_i = lax.broadcasted_iota(jnp.int32, (TILE, TILE), 1)
    anti = jnp.where(a_i + b_i == TILE - 1, 1.0, 0.0).astype(jnp.bfloat16)

    def one_channel(c, carry):
        s_t = x_ref[:, 0, 0, c, :, :].reshape(src * t16, width)
        r_t = x_ref[:, 1, 0, c, :, :].reshape(src * t16, width)
        swapped = jnp.concatenate([r_t[:, TILE:], r_t[:, :TILE]], axis=0)
        rev = jnp.dot(swapped, anti, preferred_element_type=jnp.float32).astype(jnp.bfloat16)
        r_t = jnp.concatenate([rev[:src * t16], rev[src * t16:]], axis=1)
        g = lax.dot_general(s_t, r_t, (((0,), (0,)), ((), ())),
                            preferred_element_type=jnp.float32)
        q = pltpu.roll(g, 2 * half + 1, 1, stride=1, stride_axis=0)
        q = jnp.where(v_ok, q, 0.0)
        band_ref[...] = q[:, :TILE].T[:rows, :]
        for j in range(LAGS):
            d = half - j
            w = band_ref[2 * j:2 * j + 1, :]
            out = pltpu.roll(w, d % width, 1)
            out = jnp.where((x_i - d >= 0) & (x_i - d < width), out, 0.0)
            o_ref[0, 0, c, pl.ds(half + d, 1), :] = out[:, :TILE]
            o_ref[0, 1, c, pl.ds(half + d, 1), :] = out[:, TILE:]
        return carry

    lax.fori_loop(0, cb, one_channel, 0, unroll=2)


def lag_images(pair):
    n_src, _, shots, chans, t16, width = pair.shape
    cb = min(CB, chans)
    return pl.pallas_call(
        lag_kernel,
        grid=(shots, chans // cb),
        in_specs=[pl.BlockSpec((n_src, 2, 1, cb, t16, width), lambda i, j: (0, 0, i, j, 0, 0))],
        out_specs=pl.BlockSpec((1, 2, cb, LAGS, TILE), lambda i, j: (i, 0, j, 0, 0)),
        out_shape=jax.ShapeDtypeStruct((shots, 2, chans, LAGS, TILE), jnp.float32),
        scratch_shapes=[pltpu.VMEM((72, width), jnp.float32)],
    )(pair)


def place_tiles(image, first, base, slots):
    shots = image.shape[0]
    target = first[:, None] + jnp.arange(2, dtype=jnp.int32)[None, :] - base
    out = []
    for k in range(slots):
        acc = None
        for s in range(shots):
            for a in range(2):
                term = jnp.where(target[s, a] == k, image[s, a], 0.0)
                acc = term if acc is None else acc + term
        out.append(acc)
    return out


def body(source_snap, receiver_snap, start_tile):
    owner = lax.axis_index("space")
    images = []
    received = []
    first = 0
    for g, size in enumerate(CHUNKS):
        cs = slice(first, first + size)
        first += size
        pair = jnp.stack([source_snap[:, :, cs], receiver_snap[:, :, cs]])
        pair = jnp.transpose(pair, (4, 0, 1, 3, 2, 5))
        if g >= 1:
            pair, received[g - 1] = lax.optimization_barrier((pair, received[g - 1]))
        if g >= 2:
            pair, images[g - 2] = lax.optimization_barrier((pair, images[g - 2]))
        received.append(lax.all_to_all(pair, "tm", split_axis=0, concat_axis=0, tiled=True))
        if g >= 1:
            images.append(lag_images(received[g - 1]))
    early = [place_tiles(image, start_tile, owner - 1, 3) for image in images]
    early = [jnp.concatenate([p[k] for p in early], axis=0) for k in range(3)]
    early, received[-1] = lax.optimization_barrier((early, received[-1]))
    parts = [early, place_tiles(lag_images(received[-1]), start_tile, owner - 1, 3)]
    out = []
    for slots in parts:
        right_part = passed_along(slots[0], "space", -1)
        left_part = passed_along(slots[2], "space", 1)
        out.append(slots[1] + right_part + left_part)
    return jnp.concatenate(out, axis=0)[None]


def solution(mesh):
    in_specs = (P("space", "tm", None, None, None), P("space", "tm", None, None, None), P("space"))
    out_specs = P("tm", None, None, "space")
    return jax.shard_map(body, mesh=mesh, in_specs=in_specs, out_specs=out_specs, check_vma=False)
```

```python
import functools

import jax
import jax.numpy as jnp
from jax import lax
from jax.experimental import pallas as pl
from jax.experimental.pallas import tpu as pltpu
from jax.sharding import PartitionSpec as P

LAGS = 33
TILE = 128
CB = 8
CHUNKS = (8, 40, 16)


def passed_along(block, axis, distance):
    devices = range(lax.axis_size(axis))
    route = [(i - distance, i) for i in devices if i - distance in devices]
    return lax.ppermute(block, axis, route)


def lag_kernel(x_ref, o_ref, band_ref):
    src, _, _, cb, t16, width = x_ref.shape
    half = (LAGS - 1) // 2
    rows = band_ref.shape[0]
    u_i = lax.broadcasted_iota(jnp.int32, (width, width), 0)
    k_i = lax.broadcasted_iota(jnp.int32, (width, width), 1)
    v_ok = (u_i - k_i + 2 * half >= 0) & (u_i - k_i + 2 * half < width)
    x_i = lax.broadcasted_iota(jnp.int32, (cb, width), 1)
    a_i = lax.broadcasted_iota(jnp.int32, (TILE, TILE), 0)
    b_i = lax.broadcasted_iota(jnp.int32, (TILE, TILE), 1)
    anti = jnp.where(a_i + b_i == TILE - 1, 1.0, 0.0).astype(jnp.bfloat16)

    for c in range(cb):
        s_t = x_ref[:, 0, 0, c, :, :].reshape(src * t16, width)
        r_t = x_ref[:, 1, 0, c, :, :].reshape(src * t16, width)
        swapped = jnp.concatenate([r_t[:, TILE:], r_t[:, :TILE]], axis=0)
        rev = jnp.dot(swapped, anti, preferred_element_type=jnp.float32).astype(jnp.bfloat16)
        r_t = jnp.concatenate([rev[:src * t16], rev[src * t16:]], axis=1)
        g = lax.dot_general(s_t, r_t, (((0,), (0,)), ((), ())),
                            preferred_element_type=jnp.float32)
        q = pltpu.roll(g, 2 * half + 1, 1, stride=1, stride_axis=0)
        q = jnp.where(v_ok, q, 0.0)
        band_ref[:, c, :] = q[:, :TILE].T[:rows, :]
    for j in range(LAGS):
        d = half - j
        w = band_ref[2 * j]
        out = pltpu.roll(w, d % width, 1)
        out = jnp.where((x_i - d >= 0) & (x_i - d < width), out, 0.0)
        o_ref[0, 0, half + d] = out[:, :TILE]
        o_ref[0, 1, half + d] = out[:, TILE:]


def lag_images(pair):
    n_src, _, shots, chans, t16, width = pair.shape
    cb = min(CB, chans)
    return pl.pallas_call(
        lag_kernel,
        grid=(shots, chans // cb),
        in_specs=[pl.BlockSpec((n_src, 2, 1, cb, t16, width), lambda i, j: (0, 0, i, j, 0, 0))],
        out_specs=pl.BlockSpec((1, 2, LAGS, cb, TILE), lambda i, j: (i, 0, 0, j, 0)),
        out_shape=jax.ShapeDtypeStruct((shots, 2, LAGS, chans, TILE), jnp.float32),
        scratch_shapes=[pltpu.VMEM((72, cb, width), jnp.float32)],
    )(pair)


def place_tiles(image, first, base, slots):
    shots = image.shape[0]
    target = first[:, None] + jnp.arange(2, dtype=jnp.int32)[None, :] - base
    out = []
    for k in range(slots):
        acc = None
        for s in range(shots):
            for a in range(2):
                term = jnp.where(target[s, a] == k, image[s, a], 0.0)
                acc = term if acc is None else acc + term
        out.append(acc)
    return out


def body(source_snap, receiver_snap, start_tile):
    owner = lax.axis_index("space")
    images = []
    received = []
    first = 0
    for g, size in enumerate(CHUNKS):
        cs = slice(first, first + size)
        first += size
        pair = jnp.stack([source_snap[:, :, cs], receiver_snap[:, :, cs]])
        pair = jnp.transpose(pair, (4, 0, 1, 3, 2, 5))
        if g >= 1:
            pair, received[g - 1] = lax.optimization_barrier((pair, received[g - 1]))
        if g >= 2:
            pair, images[g - 2] = lax.optimization_barrier((pair, images[g - 2]))
        received.append(lax.all_to_all(pair, "tm", split_axis=0, concat_axis=0, tiled=True))
        if g >= 1:
            images.append(lag_images(received[g - 1]))
    early = [place_tiles(image, start_tile, owner - 1, 3) for image in images]
    early = [jnp.concatenate([p[k] for p in early], axis=1) for k in range(3)]
    early, received[-1] = lax.optimization_barrier((early, received[-1]))
    parts = [early, place_tiles(lag_images(received[-1]), start_tile, owner - 1, 3)]
    out = []
    for slots in parts:
        right_part = passed_along(slots[0], "space", -1)
        left_part = passed_along(slots[2], "space", 1)
        out.append(slots[1] + right_part + left_part)
    return jnp.transpose(jnp.concatenate(out, axis=1), (1, 0, 2))[None]


def solution(mesh):
    in_specs = (P("space", "tm", None, None, None), P("space", "tm", None, None, None), P("space"))
    out_specs = P("tm", None, None, "space")
    return jax.shard_map(body, mesh=mesh, in_specs=in_specs, out_specs=out_specs, check_vma=False)
```

```python
import functools

import jax
import jax.numpy as jnp
from jax import lax
from jax.experimental import pallas as pl
from jax.experimental.pallas import tpu as pltpu
from jax.sharding import PartitionSpec as P

LAGS = 33
TILE = 128
CB = 8
CHUNKS = (8, 48, 8)


def passed_along(block, axis, distance):
    devices = range(lax.axis_size(axis))
    route = [(i - distance, i) for i in devices if i - distance in devices]
    return lax.ppermute(block, axis, route)


def lag_kernel(x_ref, o_ref, band_ref):
    src, _, _, cb, t16, width = x_ref.shape
    half = (LAGS - 1) // 2
    rows = band_ref.shape[0]
    u_i = lax.broadcasted_iota(jnp.int32, (width, width), 0)
    k_i = lax.broadcasted_iota(jnp.int32, (width, width), 1)
    v_ok = (u_i - k_i + 2 * half >= 0) & (u_i - k_i + 2 * half < width)
    x_i = lax.broadcasted_iota(jnp.int32, (cb, width), 1)
    a_i = lax.broadcasted_iota(jnp.int32, (TILE, TILE), 0)
    b_i = lax.broadcasted_iota(jnp.int32, (TILE, TILE), 1)
    anti = jnp.where(a_i + b_i == TILE - 1, 1.0, 0.0).astype(jnp.bfloat16)

    for c in range(cb):
        s_t = x_ref[:, 0, 0, c, :, :].reshape(src * t16, width)
        r_t = x_ref[:, 1, 0, c, :, :].reshape(src * t16, width)
        swapped = jnp.concatenate([r_t[:, TILE:], r_t[:, :TILE]], axis=0)
        rev = jnp.dot(swapped, anti, preferred_element_type=jnp.float32).astype(jnp.bfloat16)
        r_t = jnp.concatenate([rev[:src * t16], rev[src * t16:]], axis=1)
        g = lax.dot_general(s_t, r_t, (((0,), (0,)), ((), ())),
                            preferred_element_type=jnp.float32)
        q = pltpu.roll(g, 2 * half + 1, 1, stride=1, stride_axis=0)
        q = jnp.where(v_ok, q, 0.0)
        band_ref[:, c, :] = q[:, :TILE].T[:rows, :]
    for j in range(LAGS):
        d = half - j
        w = band_ref[2 * j]
        out = pltpu.roll(w, d % width, 1)
        out = jnp.where((x_i - d >= 0) & (x_i - d < width), out, 0.0)
        o_ref[0, 0, half + d] = out[:, :TILE]
        o_ref[0, 1, half + d] = out[:, TILE:]


def lag_images(pair):
    n_src, _, shots, chans, t16, width = pair.shape
    cb = min(CB, chans)
    return pl.pallas_call(
        lag_kernel,
        grid=(shots, chans // cb),
        in_specs=[pl.BlockSpec((n_src, 2, 1, cb, t16, width), lambda i, j: (0, 0, i, j, 0, 0))],
        out_specs=pl.BlockSpec((1, 2, LAGS, cb, TILE), lambda i, j: (i, 0, 0, j, 0)),
        out_shape=jax.ShapeDtypeStruct((shots, 2, LAGS, chans, TILE), jnp.float32),
        scratch_shapes=[pltpu.VMEM((72, cb, width), jnp.float32)],
    )(pair)


def place_tiles(image, first, base, slots):
    shots = image.shape[0]
    target = first[:, None] + jnp.arange(2, dtype=jnp.int32)[None, :] - base
    out = []
    for k in range(slots):
        acc = None
        for s in range(shots):
            for a in range(2):
                term = jnp.where(target[s, a] == k, image[s, a], 0.0)
                acc = term if acc is None else acc + term
        out.append(acc)
    return out


def body(source_snap, receiver_snap, start_tile):
    owner = lax.axis_index("space")
    images = []
    received = []
    first = 0
    for g, size in enumerate(CHUNKS):
        cs = slice(first, first + size)
        first += size
        pair = jnp.stack([source_snap[:, :, cs], receiver_snap[:, :, cs]])
        pair = jnp.transpose(pair, (4, 0, 1, 3, 2, 5))
        if g >= 1:
            pair, received[g - 1] = lax.optimization_barrier((pair, received[g - 1]))
        if g >= 2:
            pair, images[g - 2] = lax.optimization_barrier((pair, images[g - 2]))
        received.append(lax.all_to_all(pair, "tm", split_axis=0, concat_axis=0, tiled=True))
        if g >= 1:
            images.append(lag_images(received[g - 1]))
    early = [place_tiles(image, start_tile, owner - 1, 3) for image in images]
    early = [jnp.concatenate([p[k] for p in early], axis=1) for k in range(3)]
    early, received[-1] = lax.optimization_barrier((early, received[-1]))
    parts = [early, place_tiles(lag_images(received[-1]), start_tile, owner - 1, 3)]
    out = []
    for slots in parts:
        right_part = passed_along(slots[0], "space", -1)
        left_part = passed_along(slots[2], "space", 1)
        out.append(slots[1] + right_part + left_part)
    return jnp.transpose(jnp.concatenate(out, axis=1), (1, 0, 2))[None]


def solution(mesh):
    in_specs = (P("space", "tm", None, None, None), P("space", "tm", None, None, None), P("space"))
    out_specs = P("tm", None, None, "space")
    return jax.shard_map(body, mesh=mesh, in_specs=in_specs, out_specs=out_specs, check_vma=False)
```

```python
import functools

import jax
import jax.numpy as jnp
from jax import lax
from jax.experimental import pallas as pl
from jax.experimental.pallas import tpu as pltpu
from jax.sharding import PartitionSpec as P

LAGS = 33
TILE = 128
CB = 8
CHUNKS = (8, 40, 16)


def passed_along(block, axis, distance):
    devices = range(lax.axis_size(axis))
    route = [(i - distance, i) for i in devices if i - distance in devices]
    return lax.ppermute(block, axis, route)


def lag_kernel(x_ref, o_ref, band_ref):
    src, _, _, cb, t16, width = x_ref.shape
    half = (LAGS - 1) // 2
    rows = band_ref.shape[0]
    u_i = lax.broadcasted_iota(jnp.int32, (width, width), 0)
    k_i = lax.broadcasted_iota(jnp.int32, (width, width), 1)
    v_ok = (u_i - k_i + 2 * half >= 0) & (u_i - k_i + 2 * half < width)
    x_i = lax.broadcasted_iota(jnp.int32, (cb, width), 1)
    a_i = lax.broadcasted_iota(jnp.int32, (TILE, TILE), 0)
    b_i = lax.broadcasted_iota(jnp.int32, (TILE, TILE), 1)
    anti = jnp.where(a_i + b_i == TILE - 1, 1.0, 0.0).astype(jnp.bfloat16)

    for c in range(cb):
        s_t = x_ref[:, 0, 0, c, :, :].reshape(src * t16, width)
        r_t = x_ref[:, 1, 0, c, :, :].reshape(src * t16, width)
        swapped = jnp.concatenate([r_t[:, TILE:], r_t[:, :TILE]], axis=0)
        rev = jnp.dot(swapped, anti, preferred_element_type=jnp.float32).astype(jnp.bfloat16)
        r_t = jnp.concatenate([rev[:src * t16], rev[src * t16:]], axis=1)
        g = lax.dot_general(s_t, r_t, (((0,), (0,)), ((), ())),
                            preferred_element_type=jnp.float32)
        q = pltpu.roll(g, 2 * half + 1, 1, stride=1, stride_axis=0)
        q = jnp.where(v_ok, q, 0.0)
        band_ref[:, c, :] = q[:, :TILE].T[:rows, :]
    for j in range(LAGS):
        d = half - j
        w = band_ref[2 * j]
        out = pltpu.roll(w, d % width, 1)
        out = jnp.where((x_i - d >= 0) & (x_i - d < width), out, 0.0)
        o_ref[0, 0, half + d] = out[:, :TILE]
        o_ref[0, 1, half + d] = out[:, TILE:]


def lag_images(pair):
    n_src, _, shots, chans, t16, width = pair.shape
    cb = min(CB, chans)
    return pl.pallas_call(
        lag_kernel,
        grid=(shots, chans // cb),
        in_specs=[pl.BlockSpec((n_src, 2, 1, cb, t16, width), lambda i, j: (0, 0, i, j, 0, 0))],
        out_specs=pl.BlockSpec((1, 2, LAGS, cb, TILE), lambda i, j: (i, 0, 0, j, 0)),
        out_shape=jax.ShapeDtypeStruct((shots, 2, LAGS, chans, TILE), jnp.float32),
        scratch_shapes=[pltpu.VMEM((72, cb, width), jnp.float32)],
    )(pair)


def place_tiles(image, first, base, slots):
    shots = image.shape[0]
    target = first[:, None] + jnp.arange(2, dtype=jnp.int32)[None, :] - base
    out = []
    for k in range(slots):
        acc = None
        for s in range(shots):
            for a in range(2):
                term = jnp.where(target[s, a] == k, image[s, a], 0.0)
                acc = term if acc is None else acc + term
        out.append(acc)
    return out


def body(source_snap, receiver_snap, start_tile):
    owner = lax.axis_index("space")
    images = []
    received = []
    first = 0
    for g, size in enumerate(CHUNKS):
        cs = slice(first, first + size)
        first += size
        pair = jnp.stack([source_snap[:, :, cs], receiver_snap[:, :, cs]])
        pair = jnp.transpose(pair, (4, 0, 1, 3, 2, 5))
        if g >= 1:
            pair, received[g - 1] = lax.optimization_barrier((pair, received[g - 1]))
        if g >= 2:
            pair, images[g - 2] = lax.optimization_barrier((pair, images[g - 2]))
        received.append(lax.all_to_all(pair, "tm", split_axis=0, concat_axis=0, tiled=True))
        if g >= 1:
            images.append(lag_images(received[g - 1]))
    early = [place_tiles(image, start_tile, owner - 1, 3) for image in images]
    early = [jnp.concatenate([p[k] for p in early], axis=1) for k in range(3)]
    parts = [early, place_tiles(lag_images(received[-1]), start_tile, owner - 1, 3)]
    out = []
    for slots in parts:
        right_part = passed_along(slots[0], "space", -1)
        left_part = passed_along(slots[2], "space", 1)
        out.append(slots[1] + right_part + left_part)
    return jnp.transpose(jnp.concatenate(out, axis=1), (1, 0, 2))[None]


def solution(mesh):
    in_specs = (P("space", "tm", None, None, None), P("space", "tm", None, None, None), P("space"))
    out_specs = P("tm", None, None, "space")
    return jax.shard_map(body, mesh=mesh, in_specs=in_specs, out_specs=out_specs, check_vma=False)
```

```python
import functools

import jax
import jax.numpy as jnp
from jax import lax
from jax.experimental import pallas as pl
from jax.experimental.pallas import tpu as pltpu
from jax.sharding import PartitionSpec as P

LAGS = 33
TILE = 128
CB = 8
CHUNKS = (8, 40, 16)


def passed_along(block, axis, distance):
    devices = range(lax.axis_size(axis))
    route = [(i - distance, i) for i in devices if i - distance in devices]
    return lax.ppermute(block, axis, route)


def lag_kernel(x_ref, o_ref, band_ref):
    src, _, _, cb, t16, width = x_ref.shape
    half = (LAGS - 1) // 2
    rows = band_ref.shape[0]
    u_i = lax.broadcasted_iota(jnp.int32, (width, width), 0)
    k_i = lax.broadcasted_iota(jnp.int32, (width, width), 1)
    v_ok = (u_i - k_i + 2 * half >= 0) & (u_i - k_i + 2 * half < width)
    x_i = lax.broadcasted_iota(jnp.int32, (cb, width), 1)
    a_i = lax.broadcasted_iota(jnp.int32, (TILE, TILE), 0)
    b_i = lax.broadcasted_iota(jnp.int32, (TILE, TILE), 1)
    anti = jnp.where(a_i + b_i == TILE - 1, 1.0, 0.0).astype(jnp.bfloat16)

    for c in range(cb):
        s_t = x_ref[:, 0, 0, c, :, :].reshape(src * t16, width)
        r_t = x_ref[:, 1, 0, c, :, :].reshape(src * t16, width)
        swapped = jnp.concatenate([r_t[:, TILE:], r_t[:, :TILE]], axis=0)
        rev = jnp.dot(swapped, anti, preferred_element_type=jnp.float32).astype(jnp.bfloat16)
        r_t = jnp.concatenate([rev[:src * t16], rev[src * t16:]], axis=1)
        g = lax.dot_general(s_t, r_t, (((0,), (0,)), ((), ())),
                            preferred_element_type=jnp.float32)
        q = pltpu.roll(g, 2 * half + 1, 1, stride=1, stride_axis=0)
        q = jnp.where(v_ok, q, 0.0)
        band_ref[:, c, :] = q[:, :TILE].T[:rows, :]
    for j in range(LAGS):
        d = half - j
        w = band_ref[2 * j]
        out = pltpu.roll(w, d % width, 1)
        out = jnp.where((x_i - d >= 0) & (x_i - d < width), out, 0.0)
        o_ref[0, 0, half + d] = out[:, :TILE]
        o_ref[0, 1, half + d] = out[:, TILE:]


def lag_images(pair):
    n_src, _, shots, chans, t16, width = pair.shape
    cb = 2 * CB if chans % (2 * CB) == 0 else min(CB, chans)
    return pl.pallas_call(
        lag_kernel,
        grid=(shots, chans // cb),
        in_specs=[pl.BlockSpec((n_src, 2, 1, cb, t16, width), lambda i, j: (0, 0, i, j, 0, 0))],
        out_specs=pl.BlockSpec((1, 2, LAGS, cb, TILE), lambda i, j: (i, 0, 0, j, 0)),
        out_shape=jax.ShapeDtypeStruct((shots, 2, LAGS, chans, TILE), jnp.float32),
        scratch_shapes=[pltpu.VMEM((72, cb, width), jnp.float32)],
    )(pair)


def place_tiles(image, first, base, slots):
    shots = image.shape[0]
    target = first[:, None] + jnp.arange(2, dtype=jnp.int32)[None, :] - base
    out = []
    for k in range(slots):
        acc = None
        for s in range(shots):
            for a in range(2):
                term = jnp.where(target[s, a] == k, image[s, a], 0.0)
                acc = term if acc is None else acc + term
        out.append(acc)
    return out


def body(source_snap, receiver_snap, start_tile):
    owner = lax.axis_index("space")
    images = []
    received = []
    first = 0
    for g, size in enumerate(CHUNKS):
        cs = slice(first, first + size)
        first += size
        pair = jnp.stack([source_snap[:, :, cs], receiver_snap[:, :, cs]])
        pair = jnp.transpose(pair, (4, 0, 1, 3, 2, 5))
        if g >= 1:
            pair, received[g - 1] = lax.optimization_barrier((pair, received[g - 1]))
        if g >= 2:
            pair, images[g - 2] = lax.optimization_barrier((pair, images[g - 2]))
        received.append(lax.all_to_all(pair, "tm", split_axis=0, concat_axis=0, tiled=True))
        if g >= 1:
            images.append(lag_images(received[g - 1]))
    early = [place_tiles(image, start_tile, owner - 1, 3) for image in images]
    early = [jnp.concatenate([p[k] for p in early], axis=1) for k in range(3)]
    early, received[-1] = lax.optimization_barrier((early, received[-1]))
    parts = [early, place_tiles(lag_images(received[-1]), start_tile, owner - 1, 3)]
    out = []
    for slots in parts:
        right_part = passed_along(slots[0], "space", -1)
        left_part = passed_along(slots[2], "space", 1)
        out.append(slots[1] + right_part + left_part)
    return jnp.transpose(jnp.concatenate(out, axis=1), (1, 0, 2))[None]


def solution(mesh):
    in_specs = (P("space", "tm", None, None, None), P("space", "tm", None, None, None), P("space"))
    out_specs = P("tm", None, None, "space")
    return jax.shard_map(body, mesh=mesh, in_specs=in_specs, out_specs=out_specs, check_vma=False)
```

```python
import functools

import jax
import jax.numpy as jnp
from jax import lax
from jax.experimental import pallas as pl
from jax.experimental.pallas import tpu as pltpu
from jax.sharding import PartitionSpec as P

LAGS = 33
TILE = 128
CB = 8
CHUNKS = (16, 40, 8)


def passed_along(block, axis, distance):
    devices = range(lax.axis_size(axis))
    route = [(i - distance, i) for i in devices if i - distance in devices]
    return lax.ppermute(block, axis, route)


def lag_kernel(x_ref, o_ref, band_ref):
    src, _, _, cb, t16, width = x_ref.shape
    half = (LAGS - 1) // 2
    rows = band_ref.shape[0]
    u_i = lax.broadcasted_iota(jnp.int32, (width, width), 0)
    k_i = lax.broadcasted_iota(jnp.int32, (width, width), 1)
    v_ok = (u_i - k_i + 2 * half >= 0) & (u_i - k_i + 2 * half < width)
    x_i = lax.broadcasted_iota(jnp.int32, (cb, width), 1)
    a_i = lax.broadcasted_iota(jnp.int32, (TILE, TILE), 0)
    b_i = lax.broadcasted_iota(jnp.int32, (TILE, TILE), 1)
    anti = jnp.where(a_i + b_i == TILE - 1, 1.0, 0.0).astype(jnp.bfloat16)

    for c in range(cb):
        s_t = x_ref[:, 0, 0, c, :, :].reshape(src * t16, width)
        r_t = x_ref[:, 1, 0, c, :, :].reshape(src * t16, width)
        swapped = jnp.concatenate([r_t[:, TILE:], r_t[:, :TILE]], axis=0)
        rev = jnp.dot(swapped, anti, preferred_element_type=jnp.float32).astype(jnp.bfloat16)
        r_t = jnp.concatenate([rev[:src * t16], rev[src * t16:]], axis=1)
        g = lax.dot_general(s_t, r_t, (((0,), (0,)), ((), ())),
                            preferred_element_type=jnp.float32)
        q = pltpu.roll(g, 2 * half + 1, 1, stride=1, stride_axis=0)
        q = jnp.where(v_ok, q, 0.0)
        band_ref[:, c, :] = q[:, :TILE].T[:rows, :]
    for j in range(LAGS):
        d = half - j
        w = band_ref[2 * j]
        out = pltpu.roll(w, d % width, 1)
        out = jnp.where((x_i - d >= 0) & (x_i - d < width), out, 0.0)
        o_ref[0, 0, half + d] = out[:, :TILE]
        o_ref[0, 1, half + d] = out[:, TILE:]


def lag_images(pair):
    n_src, _, shots, chans, t16, width = pair.shape
    cb = min(CB, chans)
    return pl.pallas_call(
        lag_kernel,
        grid=(shots, chans // cb),
        in_specs=[pl.BlockSpec((n_src, 2, 1, cb, t16, width), lambda i, j: (0, 0, i, j, 0, 0))],
        out_specs=pl.BlockSpec((1, 2, LAGS, cb, TILE), lambda i, j: (i, 0, 0, j, 0)),
        out_shape=jax.ShapeDtypeStruct((shots, 2, LAGS, chans, TILE), jnp.float32),
        scratch_shapes=[pltpu.VMEM((72, cb, width), jnp.float32)],
    )(pair)


def place_tiles(image, first, base, slots):
    shots = image.shape[0]
    target = first[:, None] + jnp.arange(2, dtype=jnp.int32)[None, :] - base
    out = []
    for k in range(slots):
        acc = None
        for s in range(shots):
            for a in range(2):
                term = jnp.where(target[s, a] == k, image[s, a], 0.0)
                acc = term if acc is None else acc + term
        out.append(acc)
    return out


def body(source_snap, receiver_snap, start_tile):
    owner = lax.axis_index("space")
    images = []
    received = []
    first = 0
    for g, size in enumerate(CHUNKS):
        cs = slice(first, first + size)
        first += size
        pair = jnp.stack([source_snap[:, :, cs], receiver_snap[:, :, cs]])
        pair = jnp.transpose(pair, (4, 0, 1, 3, 2, 5))
        if g >= 1:
            pair, received[g - 1] = lax.optimization_barrier((pair, received[g - 1]))
        if g >= 2:
            pair, images[g - 2] = lax.optimization_barrier((pair, images[g - 2]))
        received.append(lax.all_to_all(pair, "tm", split_axis=0, concat_axis=0, tiled=True))
        if g >= 1:
            images.append(lag_images(received[g - 1]))
    early = [place_tiles(image, start_tile, owner - 1, 3) for image in images]
    early = [jnp.concatenate([p[k] for p in early], axis=1) for k in range(3)]
    early, received[-1] = lax.optimization_barrier((early, received[-1]))
    parts = [early, place_tiles(lag_images(received[-1]), start_tile, owner - 1, 3)]
    out = []
    for slots in parts:
        right_part = passed_along(slots[0], "space", -1)
        left_part = passed_along(slots[2], "space", 1)
        out.append(slots[1] + right_part + left_part)
    return jnp.transpose(jnp.concatenate(out, axis=1), (1, 0, 2))[None]


def solution(mesh):
    in_specs = (P("space", "tm", None, None, None), P("space", "tm", None, None, None), P("space"))
    out_specs = P("tm", None, None, "space")
    return jax.shard_map(body, mesh=mesh, in_specs=in_specs, out_specs=out_specs, check_vma=False)
```

```python
import functools

import jax
import jax.numpy as jnp
from jax import lax
from jax.experimental import pallas as pl
from jax.experimental.pallas import tpu as pltpu
from jax.sharding import PartitionSpec as P

LAGS = 33
TILE = 128
CB = 8
CHUNKS = (16, 32, 16)


def passed_along(block, axis, distance):
    devices = range(lax.axis_size(axis))
    route = [(i - distance, i) for i in devices if i - distance in devices]
    return lax.ppermute(block, axis, route)


def lag_kernel(x_ref, o_ref, band_ref):
    src, _, _, cb, t16, width = x_ref.shape
    half = (LAGS - 1) // 2
    rows = band_ref.shape[0]
    u_i = lax.broadcasted_iota(jnp.int32, (width, width), 0)
    k_i = lax.broadcasted_iota(jnp.int32, (width, width), 1)
    v_ok = (u_i - k_i + 2 * half >= 0) & (u_i - k_i + 2 * half < width)
    x_i = lax.broadcasted_iota(jnp.int32, (cb, width), 1)
    a_i = lax.broadcasted_iota(jnp.int32, (TILE, TILE), 0)
    b_i = lax.broadcasted_iota(jnp.int32, (TILE, TILE), 1)
    anti = jnp.where(a_i + b_i == TILE - 1, 1.0, 0.0).astype(jnp.bfloat16)

    for c in range(cb):
        s_t = x_ref[:, 0, 0, c, :, :].reshape(src * t16, width)
        r_t = x_ref[:, 1, 0, c, :, :].reshape(src * t16, width)
        swapped = jnp.concatenate([r_t[:, TILE:], r_t[:, :TILE]], axis=0)
        rev = jnp.dot(swapped, anti, preferred_element_type=jnp.float32).astype(jnp.bfloat16)
        r_t = jnp.concatenate([rev[:src * t16], rev[src * t16:]], axis=1)
        g = lax.dot_general(s_t, r_t, (((0,), (0,)), ((), ())),
                            preferred_element_type=jnp.float32)
        q = pltpu.roll(g, 2 * half + 1, 1, stride=1, stride_axis=0)
        q = jnp.where(v_ok, q, 0.0)
        band_ref[:, c, :] = q[:, :TILE].T[:rows, :]
    for j in range(LAGS):
        d = half - j
        w = band_ref[2 * j]
        out = pltpu.roll(w, d % width, 1)
        out = jnp.where((x_i - d >= 0) & (x_i - d < width), out, 0.0)
        o_ref[0, 0, half + d] = out[:, :TILE]
        o_ref[0, 1, half + d] = out[:, TILE:]


def lag_images(pair):
    n_src, _, shots, chans, t16, width = pair.shape
    cb = min(CB, chans)
    return pl.pallas_call(
        lag_kernel,
        grid=(shots, chans // cb),
        in_specs=[pl.BlockSpec((n_src, 2, 1, cb, t16, width), lambda i, j: (0, 0, i, j, 0, 0))],
        out_specs=pl.BlockSpec((1, 2, LAGS, cb, TILE), lambda i, j: (i, 0, 0, j, 0)),
        out_shape=jax.ShapeDtypeStruct((shots, 2, LAGS, chans, TILE), jnp.float32),
        scratch_shapes=[pltpu.VMEM((72, cb, width), jnp.float32)],
    )(pair)


def place_tiles(image, first, base, slots):
    shots = image.shape[0]
    target = first[:, None] + jnp.arange(2, dtype=jnp.int32)[None, :] - base
    out = []
    for k in range(slots):
        acc = None
        for s in range(shots):
            for a in range(2):
                term = jnp.where(target[s, a] == k, image[s, a], 0.0)
                acc = term if acc is None else acc + term
        out.append(acc)
    return out


def body(source_snap, receiver_snap, start_tile):
    owner = lax.axis_index("space")
    images = []
    received = []
    first = 0
    for g, size in enumerate(CHUNKS):
        cs = slice(first, first + size)
        first += size
        pair = jnp.stack([source_snap[:, :, cs], receiver_snap[:, :, cs]])
        pair = jnp.transpose(pair, (4, 0, 1, 3, 2, 5))
        if g >= 1:
            pair, received[g - 1] = lax.optimization_barrier((pair, received[g - 1]))
        if g >= 2:
            pair, images[g - 2] = lax.optimization_barrier((pair, images[g - 2]))
        received.append(lax.all_to_all(pair, "tm", split_axis=0, concat_axis=0, tiled=True))
        if g >= 1:
            images.append(lag_images(received[g - 1]))
    early = [place_tiles(image, start_tile, owner - 1, 3) for image in images]
    early = [jnp.concatenate([p[k] for p in early], axis=1) for k in range(3)]
    early, received[-1] = lax.optimization_barrier((early, received[-1]))
    parts = [early, place_tiles(lag_images(received[-1]), start_tile, owner - 1, 3)]
    out = []
    for slots in parts:
        right_part = passed_along(slots[0], "space", -1)
        left_part = passed_along(slots[2], "space", 1)
        out.append(slots[1] + right_part + left_part)
    return jnp.transpose(jnp.concatenate(out, axis=1), (1, 0, 2))[None]


def solution(mesh):
    in_specs = (P("space", "tm", None, None, None), P("space", "tm", None, None, None), P("space"))
    out_specs = P("tm", None, None, "space")
    return jax.shard_map(body, mesh=mesh, in_specs=in_specs, out_specs=out_specs, check_vma=False)
```
